512 devices in a mesh: seq: 64 (over z_hi, y, core), ch: 8 (over x, z_lo).
Axes of the slice: x: 4, y: 8, z: 8 (z_hi: 4, z_lo: 2; z = z_hi * 2 + z_lo), core: 2. Of those that a mesh axis runs over, the one named last changes fastest.
Arguments:
- inputs: bfloat16 [262144, 2048], P('seq', 'ch'), may hold values from -6 to 6
- first_factor: bfloat16 [512, 512], P('ch'), may hold values from -0.25 to 0.25
- twiddle: float32 [512, 512], P('seq'), may hold values from -4 to 4
- second_factor: bfloat16 [512, 512], P('ch'), may hold values from -0.25 to 0.25
- block_first: bfloat16 [64, 32, 32], P('ch'), may hold values from -1 to 1
- block_second: bfloat16 [32, 64, 64], P('ch'), may hold values from -0.75 to 0.75
Outputs:
- mixed_out: bfloat16 [262144, 2048], P('seq', 'ch')
The draws below stay inside these ranges and needn't reach their ends.
All inputs are finite; a program needn't handle non-finite values.
Results may differ from the reference program's by a relative error of at most 0.007.
Values may be sent and summed in bfloat16 or wider, within the bound.
No kernel may reach another device: no remote copies, remote signals or barrier semaphores. Data moves between devices by JAX's collectives and lax.ppermute only.
A program may use at most 128 MiB of HBM per device.

```python
import jax
import jax.numpy as jnp
from jax import lax

BLOCK = 512
CB1 = 64
CB2 = 32
D = 2048
L = 262144


def levels(rng, dims, split, smallest, high):
    level = 1.0
    for dim, shards_of in split:
        steps = jax.random.uniform(jax.random.fold_in(jax.random.fold_in(rng, 6), dim), (shards_of,), jnp.float32, smallest / len(split), high / len(split))
        level = level * jnp.repeat(jnp.exp(steps), dims[dim] // shards_of).reshape((-1,) + (1,) * (len(dims) - 1 - dim))
    return level


def centred(stream_key, dims, spread, reach, pieces=(), held_as=jnp.bfloat16):
    values = jax.random.normal(stream_key, dims, jnp.float32) * spread
    if len(pieces) > 0:
        values = levels(stream_key, dims, pieces, -0.22, 0.18) * values
    return jnp.clip(values, min=-reach, max=reach).astype(held_as)


def setup_inputs(seed: int = 0) -> dict:
    arg_keys = jax.random.split(jax.random.key(seed), 7)
    inputs = centred(arg_keys[0], (L, D), 1.0, 6.0, ((0, 64), (1, 8)))
    first_factor = centred(arg_keys[1], (BLOCK, BLOCK), BLOCK ** -0.5, 0.25, ((0, 8),))
    twiddle = centred(arg_keys[2], (BLOCK, BLOCK), 1.0, 4.0, ((0, 64),), jnp.float32)
    second_factor = centred(arg_keys[3], (BLOCK, BLOCK), BLOCK ** -0.5, 0.25, ((0, 8),))
    block_first = centred(arg_keys[4], (CB1, CB2, CB2), CB2 ** -0.5, 1.0, ((0, 8),))
    block_second = centred(arg_keys[5], (CB2, CB1, CB1), CB1 ** -0.5, 0.75, ((0, 8),))
    return {"inputs": inputs, "first_factor": first_factor, "twiddle": twiddle, "second_factor": second_factor, "block_first": block_first, "block_second": block_second}


def reference(inputs, first_factor, twiddle, second_factor, block_first, block_second):
    seq_grid = inputs.reshape(BLOCK, BLOCK, D)
    first_f32 = first_factor.astype(jnp.float32)
    second_f32 = second_factor.astype(jnp.float32)

    def group_mix(group_id):
        offset = (group_id * CB2).astype(jnp.int32)
        columns = lax.dynamic_slice_in_dim(seq_grid, offset, CB2, 2).astype(jnp.float32)
        first = jnp.einsum('kj,ijc->ikc', first_f32, columns)
        twisted = (first * twiddle[:, :, None]).astype(jnp.bfloat16)
        twisted = lax.optimization_barrier(twisted).astype(jnp.float32)
        second = jnp.einsum('pi,ikc->pkc', second_f32, twisted).astype(jnp.bfloat16)
        second = lax.optimization_barrier(second).astype(jnp.float32)
        return (columns * second).astype(jnp.bfloat16)

    stacked = lax.map(group_mix, jnp.arange(D // CB2, dtype=jnp.int32))
    gated = jnp.moveaxis(stacked, 0, 2).reshape(L, D)
    first_blocks = block_first.astype(jnp.float32)
    second_blocks = block_second.astype(jnp.float32)

    def channel_rows(row_id):
        offset = (row_id * BLOCK).astype(jnp.int32)
        rows_now = lax.dynamic_slice_in_dim(gated, offset, BLOCK, 0)
        grouped = rows_now.reshape(BLOCK, CB1, CB2).astype(jnp.float32)
        middle = jnp.einsum('amb,tab->tam', first_blocks, grouped).astype(jnp.bfloat16)
        middle = lax.optimization_barrier(middle).astype(jnp.float32)
        result_rows = jnp.einsum('mpa,tam->tmp', second_blocks, middle)
        return result_rows.reshape(BLOCK, D).astype(jnp.bfloat16)

    outputs = lax.map(channel_rows, jnp.arange(L // BLOCK, dtype=jnp.int32))
    return outputs.reshape(L, D)
```

```python
import jax
import jax.numpy as jnp
from jax import lax
from jax.sharding import PartitionSpec as P

BLOCK = 512
CHUNKS = 2


def channel_weights(block_first, block_second, n_ch):
    n_a, n_m, n_b = block_first.shape
    m_l = n_m // n_ch
    bf = jnp.transpose(block_first, (1, 0, 2))
    bf = bf.reshape(n_ch, m_l, n_a, 1, n_b)
    eye_a = jnp.eye(n_a, dtype=jnp.bool_).reshape(1, 1, n_a, n_a, 1)
    w1t = jnp.where(eye_a, bf, jnp.zeros((), bf.dtype))
    w1t = w1t.reshape(n_ch * m_l * n_a, n_a * n_b)
    n_m2, n_p, n_a2 = block_second.shape
    a_l = n_a2 // n_ch
    bs = block_second.reshape(n_m2, n_p, n_ch, a_l)
    bs = jnp.transpose(bs, (2, 0, 3, 1))
    bs = bs.reshape(n_ch, n_m2, a_l, 1, n_p)
    eye_m = jnp.eye(n_m2, dtype=jnp.bool_).reshape(1, n_m2, 1, n_m2, 1)
    w2 = jnp.where(eye_m, bs, jnp.zeros((), bs.dtype))
    w2 = w2.reshape(n_ch * n_m2 * a_l, n_m2 * n_p)
    return w1t, w2


def make_local(n_seq, n_ch):
    def local(inputs, first_factor, twiddle, second_factor, block_first, block_second):
        tok_rows, channels = inputs.shape
        outer_rows = tok_rows // BLOCK
        token_grid = inputs.reshape(outer_rows, BLOCK, channels)
        rows = first_factor.shape[0]
        both = lax.all_gather(
            jnp.concatenate([first_factor, second_factor], axis=0), "ch", axis=0, tiled=True
        ).reshape(n_ch, 2, rows, BLOCK)
        full_first = both[:, 0].reshape(BLOCK, BLOCK)
        full_second = both[:, 1].reshape(BLOCK, BLOCK)
        twiddle_t = jnp.transpose(twiddle)
        w1t, w2 = channel_weights(block_first, block_second, n_ch)
        contract = (((1,), (1,)), ((), ()))
        width = BLOCK // CHUNKS
        outs = []
        for q in range(CHUNKS):
            lo = q * width
            first = lax.dot_general(
                full_first[lo:lo + width],
                token_grid,
                contract,
                preferred_element_type=jnp.float32,
            )
            twisted = (first * twiddle_t[lo:lo + width, :, None]).astype(jnp.bfloat16)
            gathered = lax.all_to_all(twisted, "seq", split_axis=0, concat_axis=1, tiled=True)
            mixed = lax.dot_general(
                full_second, gathered, contract, preferred_element_type=jnp.float32
            ).astype(jnp.bfloat16)
            returned = lax.all_to_all(mixed, "seq", split_axis=0, concat_axis=1, tiled=True)
            gated = (
                token_grid[:, lo:lo + width].astype(jnp.float32) * returned.astype(jnp.float32)
            ).astype(jnp.bfloat16)
            gated = gated.reshape(outer_rows * width, channels)
            middle_t = lax.dot_general(
                w1t, gated, contract, preferred_element_type=jnp.float32
            ).astype(jnp.bfloat16)
            middle_t = middle_t.reshape(n_ch, channels // n_ch, outer_rows * width)
            recv = lax.all_to_all(middle_t, "ch", split_axis=0, concat_axis=0, tiled=True)
            recv = recv.reshape(channels, outer_rows * width)
            result = lax.dot_general(
                recv, w2, (((0,), (0,)), ((), ())), preferred_element_type=jnp.float32
            ).astype(jnp.bfloat16)
            outs.append(result.reshape(outer_rows, width, channels))
        out = jnp.concatenate(outs, axis=1)
        return out.reshape(tok_rows, channels)

    return local


def solution(mesh):
    placed = (
        P("seq", "ch"),
        P("ch", None),
        P("seq", None),
        P("ch", None),
        P("ch", None, None),
        P("ch", None, None),
    )
    return jax.shard_map(
        make_local(mesh.shape["seq"], mesh.shape["ch"]),
        mesh=mesh,
        in_specs=placed,
        out_specs=P("seq", "ch"),
        check_vma=False,
    )
```

```python
import jax
import jax.numpy as jnp
from jax import lax
from jax.sharding import PartitionSpec as P

BLOCK = 512
CHUNKS = 2


def channel_weights(block_first, block_second, n_ch):
    n_a, n_m, n_b = block_first.shape
    m_l = n_m // n_ch
    bf = jnp.transpose(block_first, (1, 0, 2))
    bf = bf.reshape(n_ch, m_l, n_a, 1, n_b)
    eye_a = jnp.eye(n_a, dtype=jnp.bool_).reshape(1, 1, n_a, n_a, 1)
    w1t = jnp.where(eye_a, bf, jnp.zeros((), bf.dtype))
    w1t = w1t.reshape(n_ch * m_l * n_a, n_a * n_b)
    n_m2, n_p, n_a2 = block_second.shape
    a_l = n_a2 // n_ch
    bs = block_second.reshape(n_m2, n_p, n_ch, a_l)
    bs = jnp.transpose(bs, (2, 0, 3, 1))
    bs = bs.reshape(n_ch, n_m2, a_l, 1, n_p)
    eye_m = jnp.eye(n_m2, dtype=jnp.bool_).reshape(1, n_m2, 1, n_m2, 1)
    w2 = jnp.where(eye_m, bs, jnp.zeros((), bs.dtype))
    w2 = w2.reshape(n_ch * n_m2 * a_l, n_m2 * n_p)
    return w1t, w2


def make_local(n_seq, n_ch):
    def local(inputs, first_factor, twiddle, second_factor, block_first, block_second):
        tok_rows, channels = inputs.shape
        outer_rows = tok_rows // BLOCK
        token_grid = inputs.reshape(outer_rows, BLOCK, channels)
        rows = first_factor.shape[0]
        me = lax.axis_index("ch")
        pair = jnp.concatenate([first_factor, second_factor], axis=0)
        blocks = [pair]
        for q in range(1, n_ch):
            blocks.append(
                lax.ppermute(pair, "ch", perm=[(j, (j + q) % n_ch) for j in range(n_ch)])
            )
        stacked = jnp.stack(blocks)
        order = (me - jnp.arange(n_ch)) % n_ch
        both = jnp.take(stacked, order, axis=0).reshape(n_ch, 2, rows, BLOCK)
        full_first = both[:, 0].reshape(BLOCK, BLOCK)
        full_second = both[:, 1].reshape(BLOCK, BLOCK)
        twiddle_t = jnp.transpose(twiddle)
        w1t, w2 = channel_weights(block_first, block_second, n_ch)
        w1t = jnp.take(
            w1t.reshape(n_ch, -1, channels), (me + jnp.arange(n_ch)) % n_ch, axis=0
        ).reshape(channels, channels)
        w2 = jnp.take(
            w2.reshape(n_ch, -1, channels), (me - jnp.arange(n_ch)) % n_ch, axis=0
        ).reshape(channels, channels)
        contract = (((1,), (1,)), ((), ()))
        width = BLOCK // CHUNKS
        outs = []
        for q in range(CHUNKS):
            lo = q * width
            first = lax.dot_general(
                full_first[lo:lo + width],
                token_grid,
                contract,
                preferred_element_type=jnp.float32,
            )
            twisted = (first * twiddle_t[lo:lo + width, :, None]).astype(jnp.bfloat16)
            gathered = lax.all_to_all(twisted, "seq", split_axis=0, concat_axis=1, tiled=True)
            mixed = lax.dot_general(
                full_second, gathered, contract, preferred_element_type=jnp.float32
            ).astype(jnp.bfloat16)
            returned = lax.all_to_all(mixed, "seq", split_axis=0, concat_axis=1, tiled=True)
            gated = (
                token_grid[:, lo:lo + width].astype(jnp.float32) * returned.astype(jnp.float32)
            ).astype(jnp.bfloat16)
            gated = gated.reshape(outer_rows * width, channels)
            middle_t = lax.dot_general(
                w1t, gated, contract, preferred_element_type=jnp.float32
            ).astype(jnp.bfloat16)
            middle_t = middle_t.reshape(n_ch, channels // n_ch, outer_rows * width)
            pieces = [middle_t[0]]
            for s_ in range(1, n_ch):
                pieces.append(
                    lax.ppermute(
                        middle_t[s_], "ch", perm=[(j, (j + s_) % n_ch) for j in range(n_ch)]
                    )
                )
            recv = jnp.stack(pieces).reshape(channels, outer_rows * width)
            result = lax.dot_general(
                recv, w2, (((0,), (0,)), ((), ())), preferred_element_type=jnp.float32
            ).astype(jnp.bfloat16)
            outs.append(result.reshape(outer_rows, width, channels))
        out = jnp.concatenate(outs, axis=1)
        return out.reshape(tok_rows, channels)

    return local


def solution(mesh):
    placed = (
        P("seq", "ch"),
        P("ch", None),
        P("seq", None),
        P("ch", None),
        P("ch", None, None),
        P("ch", None, None),
    )
    return jax.shard_map(
        make_local(mesh.shape["seq"], mesh.shape["ch"]),
        mesh=mesh,
        in_specs=placed,
        out_specs=P("seq", "ch"),
        check_vma=False,
    )
```

```python
import jax
import jax.numpy as jnp
from jax import lax
from jax.sharding import PartitionSpec as P

BLOCK = 512
CHUNKS = 2


def channel_weights(block_first, block_second, n_ch):
    n_a, n_m, n_b = block_first.shape
    m_l = n_m // n_ch
    bf = jnp.transpose(block_first, (1, 0, 2))
    bf = bf.reshape(n_ch, m_l, n_a, 1, n_b)
    eye_a = jnp.eye(n_a, dtype=jnp.bool_).reshape(1, 1, n_a, n_a, 1)
    w1t = jnp.where(eye_a, bf, jnp.zeros((), bf.dtype))
    w1t = w1t.reshape(n_ch * m_l * n_a, n_a * n_b)
    n_m2, n_p, n_a2 = block_second.shape
    a_l = n_a2 // n_ch
    bs = block_second.reshape(n_m2, n_p, n_ch, a_l)
    bs = jnp.transpose(bs, (2, 0, 3, 1))
    bs = bs.reshape(n_ch, n_m2, a_l, 1, n_p)
    eye_m = jnp.eye(n_m2, dtype=jnp.bool_).reshape(1, n_m2, 1, n_m2, 1)
    w2 = jnp.where(eye_m, bs, jnp.zeros((), bs.dtype))
    w2 = w2.reshape(n_ch * n_m2 * a_l, n_m2 * n_p)
    return w1t, w2


def make_local(n_seq, n_ch):
    def local(inputs, first_factor, twiddle, second_factor, block_first, block_second):
        tok_rows, channels = inputs.shape
        outer_rows = tok_rows // BLOCK
        token_grid = inputs.reshape(outer_rows, BLOCK, channels)
        rows = first_factor.shape[0]
        pair = jnp.concatenate([first_factor, second_factor], axis=0)
        spread = jnp.broadcast_to(pair[None], (n_ch,) + pair.shape)
        both = lax.all_to_all(spread, "ch", split_axis=0, concat_axis=0, tiled=True)
        both = both.reshape(n_ch, 2, rows, BLOCK)
        full_first = both[:, 0].reshape(BLOCK, BLOCK)
        full_second = both[:, 1].reshape(BLOCK, BLOCK)
        twiddle_t = jnp.transpose(twiddle)
        w1t, w2 = channel_weights(block_first, block_second, n_ch)
        contract = (((1,), (1,)), ((), ()))
        width = BLOCK // CHUNKS
        outs = []
        for q in range(CHUNKS):
            lo = q * width
            first = lax.dot_general(
                full_first[lo:lo + width],
                token_grid,
                contract,
                preferred_element_type=jnp.float32,
            )
            twisted = (first * twiddle_t[lo:lo + width, :, None]).astype(jnp.bfloat16)
            gathered = lax.all_to_all(twisted, "seq", split_axis=0, concat_axis=1, tiled=True)
            mixed = lax.dot_general(
                full_second, gathered, contract, preferred_element_type=jnp.float32
            ).astype(jnp.bfloat16)
            returned = lax.all_to_all(mixed, "seq", split_axis=0, concat_axis=1, tiled=True)
            gated = (
                token_grid[:, lo:lo + width].astype(jnp.float32) * returned.astype(jnp.float32)
            ).astype(jnp.bfloat16)
            gated = gated.reshape(outer_rows * width, channels)
            middle_t = lax.dot_general(
                w1t, gated, contract, preferred_element_type=jnp.float32
            ).astype(jnp.bfloat16)
            middle_t = middle_t.reshape(n_ch, channels // n_ch, outer_rows * width)
            recv = lax.all_to_all(middle_t, "ch", split_axis=0, concat_axis=0, tiled=True)
            recv = recv.reshape(channels, outer_rows * width)
            result = lax.dot_general(
                recv, w2, (((0,), (0,)), ((), ())), preferred_element_type=jnp.float32
            ).astype(jnp.bfloat16)
            outs.append(result.reshape(outer_rows, width, channels))
        out = jnp.concatenate(outs, axis=1)
        return out.reshape(tok_rows, channels)

    return local


def solution(mesh):
    placed = (
        P("seq", "ch"),
        P("ch", None),
        P("seq", None),
        P("ch", None),
        P("ch", None, None),
        P("ch", None, None),
    )
    return jax.shard_map(
        make_local(mesh.shape["seq"], mesh.shape["ch"]),
        mesh=mesh,
        in_specs=placed,
        out_specs=P("seq", "ch"),
        check_vma=False,
    )
```

```python
import jax
import jax.numpy as jnp
from jax import lax
from jax.sharding import Mesh, PartitionSpec as P

BLOCK = 512
CHUNKS = 2
CH = ("x", "zlo")
SPREAD = ("seq", "zlo")


def channel_weights(block_first, block_second, n_ch):
    n_a, n_m, n_b = block_first.shape
    m_l = n_m // n_ch
    bf = jnp.transpose(block_first, (1, 0, 2))
    bf = bf.reshape(n_ch, m_l, n_a, 1, n_b)
    eye_a = jnp.eye(n_a, dtype=jnp.bool_).reshape(1, 1, n_a, n_a, 1)
    w1t = jnp.where(eye_a, bf, jnp.zeros((), bf.dtype))
    w1t = w1t.reshape(n_ch * m_l * n_a, n_a * n_b)
    n_m2, n_p, n_a2 = block_second.shape
    a_l = n_a2 // n_ch
    bs = block_second.reshape(n_m2, n_p, n_ch, a_l)
    bs = jnp.transpose(bs, (2, 0, 3, 1))
    bs = bs.reshape(n_ch, n_m2, a_l, 1, n_p)
    eye_m = jnp.eye(n_m2, dtype=jnp.bool_).reshape(1, n_m2, 1, n_m2, 1)
    w2 = jnp.where(eye_m, bs, jnp.zeros((), bs.dtype))
    w2 = w2.reshape(n_ch * n_m2 * a_l, n_m2 * n_p)
    return w1t, w2


def make_local(n_seq, n_ch, n_zlo):
    def local(inputs, first_factor, twiddle, second_factor, block_first, block_second):
        tok_rows, channels = inputs.shape
        outer_rows = tok_rows // BLOCK
        token_grid = inputs.reshape(outer_rows, BLOCK, channels)
        rows = first_factor.shape[0]
        pair = jnp.concatenate([first_factor, second_factor], axis=0)
        spread = jnp.broadcast_to(pair[None], (n_ch,) + pair.shape)
        both = lax.all_to_all(spread, CH, split_axis=0, concat_axis=0, tiled=True)
        both = both.reshape(n_ch, 2, rows, BLOCK)
        full_first = both[:, 0].reshape(BLOCK, BLOCK)
        full_second = both[:, 1].reshape(BLOCK, BLOCK)
        twiddle_t = jnp.transpose(twiddle)
        w1t, w2 = channel_weights(block_first, block_second, n_ch)
        contract = (((1,), (1,)), ((), ()))
        width = BLOCK // CHUNKS
        outs = []
        for q in range(CHUNKS):
            lo = q * width
            first = lax.dot_general(
                full_first[lo:lo + width],
                token_grid,
                contract,
                preferred_element_type=jnp.float32,
            )
            twisted = (first * twiddle_t[lo:lo + width, :, None]).astype(jnp.bfloat16)
            owners = n_seq * n_zlo
            kk = width // owners
            gathered = lax.all_to_all(
                twisted.reshape(owners, kk, outer_rows, channels), SPREAD, 0, 0, tiled=True
            ).reshape(n_seq, n_zlo, kk, outer_rows, channels)
            mixed = lax.dot_general(
                full_second.reshape(BLOCK, n_seq, outer_rows),
                gathered,
                (((1, 2), (0, 3)), ((), ())),
                preferred_element_type=jnp.float32,
            ).astype(jnp.bfloat16)
            mixed = mixed.reshape(n_seq, outer_rows, n_zlo, kk, channels)
            mixed = jnp.transpose(mixed, (0, 2, 1, 3, 4)).reshape(owners, outer_rows, kk, channels)
            returned = lax.all_to_all(mixed, SPREAD, 0, 0, tiled=True)
            returned = jnp.transpose(returned, (1, 0, 2, 3)).reshape(outer_rows, width, channels)
            gated = (
                token_grid[:, lo:lo + width].astype(jnp.float32) * returned.astype(jnp.float32)
            ).astype(jnp.bfloat16)
            gated = gated.reshape(outer_rows * width, channels)
            middle_t = lax.dot_general(
                w1t, gated, contract, preferred_element_type=jnp.float32
            ).astype(jnp.bfloat16)
            middle_t = middle_t.reshape(n_ch, channels // n_ch, outer_rows * width)
            recv = lax.all_to_all(middle_t, CH, split_axis=0, concat_axis=0, tiled=True)
            recv = recv.reshape(channels, outer_rows * width)
            result = lax.dot_general(
                recv, w2, (((0,), (0,)), ((), ())), preferred_element_type=jnp.float32
            ).astype(jnp.bfloat16)
            outs.append(result.reshape(outer_rows, width, channels))
        out = jnp.concatenate(outs, axis=1)
        return out.reshape(tok_rows, channels)

    return local


def solution(mesh):
    n_seq, n_ch = mesh.shape["seq"], mesh.shape["ch"]
    n_zlo = 2
    split = Mesh(mesh.devices.reshape(n_seq, n_ch // n_zlo, n_zlo), ("seq",) + CH)
    placed = (
        P("seq", CH),
        P(CH, None),
        P("seq", None),
        P(CH, None),
        P(CH, None, None),
        P(CH, None, None),
    )
    return jax.shard_map(
        make_local(n_seq, n_ch, n_zlo),
        mesh=split,
        in_specs=placed,
        out_specs=P("seq", CH),
        check_vma=False,
    )
```

```python
import jax
import jax.numpy as jnp
from jax import lax
from jax.sharding import PartitionSpec as P

BLOCK = 512
WIDTHS = (320, 192)


def channel_weights(block_first, block_second, n_ch):
    n_a, n_m, n_b = block_first.shape
    m_l = n_m // n_ch
    bf = jnp.transpose(block_first, (1, 0, 2))
    bf = bf.reshape(n_ch, m_l, n_a, 1, n_b)
    eye_a = jnp.eye(n_a, dtype=jnp.bool_).reshape(1, 1, n_a, n_a, 1)
    w1t = jnp.where(eye_a, bf, jnp.zeros((), bf.dtype))
    w1t = w1t.reshape(n_ch * m_l * n_a, n_a * n_b)
    n_m2, n_p, n_a2 = block_second.shape
    a_l = n_a2 // n_ch
    bs = block_second.reshape(n_m2, n_p, n_ch, a_l)
    bs = jnp.transpose(bs, (2, 0, 3, 1))
    bs = bs.reshape(n_ch, n_m2, a_l, 1, n_p)
    eye_m = jnp.eye(n_m2, dtype=jnp.bool_).reshape(1, n_m2, 1, n_m2, 1)
    w2 = jnp.where(eye_m, bs, jnp.zeros((), bs.dtype))
    w2 = w2.reshape(n_ch * n_m2 * a_l, n_m2 * n_p)
    return w1t, w2


def make_local(n_seq, n_ch):
    def local(inputs, first_factor, twiddle, second_factor, block_first, block_second):
        tok_rows, channels = inputs.shape
        outer_rows = tok_rows // BLOCK
        token_grid = inputs.reshape(outer_rows, BLOCK, channels)
        rows = first_factor.shape[0]
        pair = jnp.concatenate([first_factor, second_factor], axis=0)
        spread = jnp.broadcast_to(pair[None], (n_ch,) + pair.shape)
        both = lax.all_to_all(spread, "ch", split_axis=0, concat_axis=0, tiled=True)
        both = both.reshape(n_ch, 2, rows, BLOCK)
        full_first = both[:, 0].reshape(BLOCK, BLOCK)
        full_second = both[:, 1].reshape(BLOCK, BLOCK)
        twiddle_t = jnp.transpose(twiddle)
        w1t, w2 = channel_weights(block_first, block_second, n_ch)
        contract = (((1,), (1,)), ((), ()))
        me = lax.axis_index("ch")
        w1t_rot = jnp.take(
            w1t.reshape(n_ch, -1, channels), (me + jnp.arange(n_ch)) % n_ch, axis=0
        ).reshape(channels, channels)
        w2_rot = jnp.take(
            w2.reshape(n_ch, -1, channels), (me - jnp.arange(n_ch)) % n_ch, axis=0
        ).reshape(channels, channels)

        def seq_front(lo, width):
            first = lax.dot_general(
                full_first[lo:lo + width],
                token_grid,
                contract,
                preferred_element_type=jnp.float32,
            )
            twisted = (first * twiddle_t[lo:lo + width, :, None]).astype(jnp.bfloat16)
            gathered = lax.all_to_all(twisted, "seq", split_axis=0, concat_axis=1, tiled=True)
            return lax.dot_general(
                full_second, gathered, contract, preferred_element_type=jnp.float32
            ).astype(jnp.bfloat16)

        def seq_back(mixed, lo, width, w1):
            returned = lax.all_to_all(mixed, "seq", split_axis=0, concat_axis=1, tiled=True)
            gated = (
                token_grid[:, lo:lo + width].astype(jnp.float32) * returned.astype(jnp.float32)
            ).astype(jnp.bfloat16)
            gated = gated.reshape(outer_rows * width, channels)
            middle_t = lax.dot_general(
                w1, gated, contract, preferred_element_type=jnp.float32
            ).astype(jnp.bfloat16)
            return middle_t.reshape(n_ch, channels // n_ch, outer_rows * width)

        def channel_second(recv, w, width):
            result = lax.dot_general(
                recv.reshape(channels, outer_rows * width),
                w,
                (((0,), (0,)), ((), ())),
                preferred_element_type=jnp.float32,
            ).astype(jnp.bfloat16)
            return result.reshape(outer_rows, width, channels)

        w_a, w_b = WIDTHS
        mixed_a = seq_front(0, w_a)
        mixed_b = seq_front(w_a, w_b)
        middle_a = seq_back(mixed_a, 0, w_a, w1t_rot)
        middle_a, mixed_b = lax.optimization_barrier((middle_a, mixed_b))
        pieces = [middle_a[0]]
        for q in range(1, n_ch):
            pieces.append(
                lax.ppermute(middle_a[q], "ch", perm=[(j, (j + q) % n_ch) for j in range(n_ch)])
            )
        middle_b = seq_back(mixed_b, w_a, w_b, w1t)
        recv_b = lax.all_to_all(middle_b, "ch", split_axis=0, concat_axis=0, tiled=True)
        outs = [
            channel_second(jnp.stack(pieces), w2_rot, w_a),
            channel_second(recv_b, w2, w_b),
        ]
        out = jnp.concatenate(outs, axis=1)
        return out.reshape(tok_rows, channels)

    return local


def solution(mesh):
    placed = (
        P("seq", "ch"),
        P("ch", None),
        P("seq", None),
        P("ch", None),
        P("ch", None, None),
        P("ch", None, None),
    )
    return jax.shard_map(
        make_local(mesh.shape["seq"], mesh.shape["ch"]),
        mesh=mesh,
        in_specs=placed,
        out_specs=P("seq", "ch"),
        check_vma=False,
    )
```

```python
import jax
import jax.numpy as jnp
from jax import lax
from jax.sharding import PartitionSpec as P

BLOCK = 512
CHUNKS = 1


def channel_weights(block_first, block_second, n_ch):
    n_a, n_m, n_b = block_first.shape
    m_l = n_m // n_ch
    bf = jnp.transpose(block_first, (1, 0, 2))
    bf = bf.reshape(n_ch, m_l, n_a, 1, n_b)
    eye_a = jnp.eye(n_a, dtype=jnp.bool_).reshape(1, 1, n_a, n_a, 1)
    w1t = jnp.where(eye_a, bf, jnp.zeros((), bf.dtype))
    w1t = w1t.reshape(n_ch * m_l * n_a, n_a * n_b)
    n_m2, n_p, n_a2 = block_second.shape
    a_l = n_a2 // n_ch
    bs = block_second.reshape(n_m2, n_p, n_ch, a_l)
    bs = jnp.transpose(bs, (2, 0, 3, 1))
    bs = bs.reshape(n_ch, n_m2, a_l, 1, n_p)
    eye_m = jnp.eye(n_m2, dtype=jnp.bool_).reshape(1, n_m2, 1, n_m2, 1)
    w2 = jnp.where(eye_m, bs, jnp.zeros((), bs.dtype))
    w2 = w2.reshape(n_ch * n_m2 * a_l, n_m2 * n_p)
    return w1t, w2


def make_local(n_seq, n_ch):
    def local(inputs, first_factor, twiddle, second_factor, block_first, block_second):
        tok_rows, channels = inputs.shape
        outer_rows = tok_rows // BLOCK
        token_grid = inputs.reshape(outer_rows, BLOCK, channels)
        rows = first_factor.shape[0]
        pair = jnp.concatenate([first_factor, second_factor], axis=0)
        spread = jnp.broadcast_to(pair[None], (n_ch,) + pair.shape)
        both = lax.all_to_all(spread, "ch", split_axis=0, concat_axis=0, tiled=True)
        both = both.reshape(n_ch, 2, rows, BLOCK)
        full_first = both[:, 0].reshape(BLOCK, BLOCK)
        full_second = both[:, 1].reshape(BLOCK, BLOCK)
        twiddle_t = jnp.transpose(twiddle)
        w1t, w2 = channel_weights(block_first, block_second, n_ch)
        contract = (((1,), (1,)), ((), ()))
        width = BLOCK // CHUNKS
        outs = []
        for q in range(CHUNKS):
            lo = q * width
            first = lax.dot_general(
                full_first[lo:lo + width],
                token_grid,
                contract,
                preferred_element_type=jnp.float32,
            )
            twisted = (first * twiddle_t[lo:lo + width, :, None]).astype(jnp.bfloat16)
            gathered = lax.all_to_all(twisted, "seq", split_axis=0, concat_axis=1, tiled=True)
            mixed = lax.dot_general(
                full_second, gathered, contract, preferred_element_type=jnp.float32
            ).astype(jnp.bfloat16)
            returned = lax.all_to_all(mixed, "seq", split_axis=0, concat_axis=1, tiled=True)
            gated = (
                token_grid[:, lo:lo + width].astype(jnp.float32) * returned.astype(jnp.float32)
            ).astype(jnp.bfloat16)
            gated = gated.reshape(outer_rows * width, channels)
            middle_t = lax.dot_general(
                w1t, gated, contract, preferred_element_type=jnp.float32
            ).astype(jnp.bfloat16)
            middle_t = middle_t.reshape(n_ch, channels // n_ch, outer_rows * width)
            recv = lax.all_to_all(middle_t, "ch", split_axis=0, concat_axis=0, tiled=True)
            recv = recv.reshape(channels, outer_rows * width)
            result = lax.dot_general(
                recv, w2, (((0,), (0,)), ((), ())), preferred_element_type=jnp.float32
            ).astype(jnp.bfloat16)
            outs.append(result.reshape(outer_rows, width, channels))
        out = jnp.concatenate(outs, axis=1)
        return out.reshape(tok_rows, channels)

    return local


def solution(mesh):
    placed = (
        P("seq", "ch"),
        P("ch", None),
        P("seq", None),
        P("ch", None),
        P("ch", None, None),
        P("ch", None, None),
    )
    return jax.shard_map(
        make_local(mesh.shape["seq"], mesh.shape["ch"]),
        mesh=mesh,
        in_specs=placed,
        out_specs=P("seq", "ch"),
        check_vma=False,
    )
```

```python
import jax
import jax.numpy as jnp
from jax import lax
from jax.sharding import Mesh, PartitionSpec as P

BLOCK = 512
CHUNKS = 1
SEQ = ("sq", "core")


def channel_weights(block_first, block_second, n_ch):
    n_a, n_m, n_b = block_first.shape
    m_l = n_m // n_ch
    bf = jnp.transpose(block_first, (1, 0, 2))
    bf = bf.reshape(n_ch, m_l, n_a, 1, n_b)
    eye_a = jnp.eye(n_a, dtype=jnp.bool_).reshape(1, 1, n_a, n_a, 1)
    w1t = jnp.where(eye_a, bf, jnp.zeros((), bf.dtype))
    w1t = w1t.reshape(n_ch * m_l * n_a, n_a * n_b)
    n_m2, n_p, n_a2 = block_second.shape
    a_l = n_a2 // n_ch
    bs = block_second.reshape(n_m2, n_p, n_ch, a_l)
    bs = jnp.transpose(bs, (2, 0, 3, 1))
    bs = bs.reshape(n_ch, n_m2, a_l, 1, n_p)
    eye_m = jnp.eye(n_m2, dtype=jnp.bool_).reshape(1, n_m2, 1, n_m2, 1)
    w2 = jnp.where(eye_m, bs, jnp.zeros((), bs.dtype))
    w2 = w2.reshape(n_ch * n_m2 * a_l, n_m2 * n_p)
    return w1t, w2


def make_local(n_seq, n_ch):
    def local(inputs, first_factor, twiddle, second_factor, block_first, block_second):
        tok_rows, channels = inputs.shape
        outer_rows = tok_rows // BLOCK
        token_grid = inputs.reshape(outer_rows, BLOCK, channels)
        rows = first_factor.shape[0]
        core = lax.axis_index("core")
        half = jnp.where(core == 0, first_factor, second_factor)
        spread = jnp.broadcast_to(half[None], (n_ch,) + half.shape)
        got = lax.all_to_all(spread, "ch", split_axis=0, concat_axis=0, tiled=True)
        both = lax.all_gather(got.reshape(BLOCK, BLOCK), "core", axis=0)
        full_first = both[0]
        full_second = both[1]
        twiddle_t = jnp.transpose(twiddle)
        w1t, w2 = channel_weights(block_first, block_second, n_ch)
        contract = (((1,), (1,)), ((), ()))
        width = BLOCK // CHUNKS
        outs = []
        for q in range(CHUNKS):
            lo = q * width
            first = lax.dot_general(
                full_first[lo:lo + width],
                token_grid,
                contract,
                preferred_element_type=jnp.float32,
            )
            twisted = (first * twiddle_t[lo:lo + width, :, None]).astype(jnp.bfloat16)
            gathered = lax.all_to_all(twisted, SEQ, split_axis=0, concat_axis=1, tiled=True)
            mixed = lax.dot_general(
                full_second, gathered, contract, preferred_element_type=jnp.float32
            ).astype(jnp.bfloat16)
            returned = lax.all_to_all(mixed, SEQ, split_axis=0, concat_axis=1, tiled=True)
            gated = (
                token_grid[:, lo:lo + width].astype(jnp.float32) * returned.astype(jnp.float32)
            ).astype(jnp.bfloat16)
            gated = gated.reshape(outer_rows * width, channels)
            middle_t = lax.dot_general(
                w1t, gated, contract, preferred_element_type=jnp.float32
            ).astype(jnp.bfloat16)
            middle_t = middle_t.reshape(n_ch, channels // n_ch, outer_rows * width)
            recv = lax.all_to_all(middle_t, "ch", split_axis=0, concat_axis=0, tiled=True)
            recv = recv.reshape(channels, outer_rows * width)
            result = lax.dot_general(
                recv, w2, (((0,), (0,)), ((), ())), preferred_element_type=jnp.float32
            ).astype(jnp.bfloat16)
            outs.append(result.reshape(outer_rows, width, channels))
        out = jnp.concatenate(outs, axis=1)
        return out.reshape(tok_rows, channels)

    return local


def solution(mesh):
    n_seq, n_ch = mesh.shape["seq"], mesh.shape["ch"]
    split = Mesh(mesh.devices.reshape(n_seq // 2, 2, n_ch), SEQ + ("ch",))
    placed = (
        P(SEQ, "ch"),
        P("ch", None),
        P(SEQ, None),
        P("ch", None),
        P("ch", None, None),
        P("ch", None, None),
    )
    return jax.shard_map(
        make_local(n_seq, n_ch),
        mesh=split,
        in_specs=placed,
        out_specs=P(SEQ, "ch"),
        check_vma=False,
    )
```

```python
import jax
import jax.numpy as jnp
from jax import lax
from jax.experimental import pallas as pl
from jax.sharding import PartitionSpec as P

BLOCK = 512
CHUNKS = 1


def channel_weights(block_first, block_second, n_ch):
    n_a, n_m, n_b = block_first.shape
    m_l = n_m // n_ch
    bf = jnp.transpose(block_first, (1, 0, 2))
    bf = bf.reshape(n_ch, m_l, n_a, 1, n_b)
    eye_a = jnp.eye(n_a, dtype=jnp.bool_).reshape(1, 1, n_a, n_a, 1)
    w1t = jnp.where(eye_a, bf, jnp.zeros((), bf.dtype))
    w1t = w1t.reshape(n_ch * m_l * n_a, n_a * n_b)
    n_m2, n_p, n_a2 = block_second.shape
    a_l = n_a2 // n_ch
    bs = block_second.reshape(n_m2, n_p, n_ch, a_l)
    bs = jnp.transpose(bs, (2, 0, 3, 1))
    bs = bs.reshape(n_ch, n_m2, a_l, 1, n_p)
    eye_m = jnp.eye(n_m2, dtype=jnp.bool_).reshape(1, n_m2, 1, n_m2, 1)
    w2 = jnp.where(eye_m, bs, jnp.zeros((), bs.dtype))
    w2 = w2.reshape(n_ch * n_m2 * a_l, n_m2 * n_p)
    return w1t, w2


def gate_kernel(w_ref, x_ref, r_ref, o_ref):
    srcs, _, subs, chans = r_ref.shape
    back = r_ref[:, 0, :, :].astype(jnp.float32).reshape(srcs * subs, chans)
    gated = (x_ref[0].astype(jnp.float32) * back).astype(jnp.bfloat16)
    middle = lax.dot_general(
        w_ref[...], gated, (((1,), (1,)), ((), ())), preferred_element_type=jnp.float32
    )
    o_ref[...] = middle.astype(o_ref.dtype)


def gate_first(w1t, token_grid, returned):
    outer, inner, chans = token_grid.shape
    srcs, _, subs, _ = returned.shape
    return pl.pallas_call(
        gate_kernel,
        out_shape=jax.ShapeDtypeStruct((chans, outer * inner), jnp.bfloat16),
        grid=(outer,),
        in_specs=[
            pl.BlockSpec((chans, chans), lambda p: (0, 0)),
            pl.BlockSpec((1, inner, chans), lambda p: (p, 0, 0)),
            pl.BlockSpec((srcs, 1, subs, chans), lambda p: (0, p, 0, 0)),
        ],
        out_specs=pl.BlockSpec((chans, inner), lambda p: (0, p)),
    )(w1t, token_grid, returned)


def make_local(n_seq, n_ch):
    def local(inputs, first_factor, twiddle, second_factor, block_first, block_second):
        tok_rows, channels = inputs.shape
        outer_rows = tok_rows // BLOCK
        token_grid = inputs.reshape(outer_rows, BLOCK, channels)
        rows = first_factor.shape[0]
        pair = jnp.concatenate([first_factor, second_factor], axis=0)
        spread = jnp.broadcast_to(pair[None], (n_ch,) + pair.shape)
        both = lax.all_to_all(spread, "ch", split_axis=0, concat_axis=0, tiled=True)
        both = both.reshape(n_ch, 2, rows, BLOCK)
        full_first = both[:, 0].reshape(BLOCK, BLOCK)
        full_second = both[:, 1].reshape(BLOCK, BLOCK)
        twiddle_t = jnp.transpose(twiddle)
        w1t, w2 = channel_weights(block_first, block_second, n_ch)
        contract = (((1,), (1,)), ((), ()))
        width = BLOCK // CHUNKS
        outs = []
        for q in range(CHUNKS):
            lo = q * width
            first = lax.dot_general(
                full_first[lo:lo + width],
                token_grid,
                contract,
                preferred_element_type=jnp.float32,
            )
            twisted = (first * twiddle_t[lo:lo + width, :, None]).astype(jnp.bfloat16)
            gathered = lax.all_to_all(twisted, "seq", split_axis=0, concat_axis=1, tiled=True)
            mixed = lax.dot_general(
                full_second, gathered, contract, preferred_element_type=jnp.float32
            ).astype(jnp.bfloat16)
            returned = lax.all_to_all(mixed, "seq", split_axis=0, concat_axis=0, tiled=True)
            returned = returned.reshape(n_seq, outer_rows, width // n_seq, channels)
            middle_t = gate_first(w1t, token_grid, returned)
            middle_t = middle_t.reshape(n_ch, channels // n_ch, outer_rows * width)
            recv = lax.all_to_all(middle_t, "ch", split_axis=0, concat_axis=0, tiled=True)
            recv = recv.reshape(channels, outer_rows * width)
            result = lax.dot_general(
                recv, w2, (((0,), (0,)), ((), ())), preferred_element_type=jnp.float32
            ).astype(jnp.bfloat16)
            outs.append(result.reshape(outer_rows, width, channels))
        out = jnp.concatenate(outs, axis=1)
        return out.reshape(tok_rows, channels)

    return local


def solution(mesh):
    placed = (
        P("seq", "ch"),
        P("ch", None),
        P("seq", None),
        P("ch", None),
        P("ch", None, None),
        P("ch", None, None),
    )
    return jax.shard_map(
        make_local(mesh.shape["seq"], mesh.shape["ch"]),
        mesh=mesh,
        in_specs=placed,
        out_specs=P("seq", "ch"),
        check_vma=False,
    )
```

```python
import jax
import jax.numpy as jnp
from jax import lax
from jax.experimental import pallas as pl
from jax.sharding import PartitionSpec as P

BLOCK = 512
CHUNKS = 1


def channel_weights(block_first, block_second, n_ch):
    n_a, n_m, n_b = block_first.shape
    m_l = n_m // n_ch
    bf = jnp.transpose(block_first, (1, 0, 2))
    bf = bf.reshape(n_ch, m_l, n_a, 1, n_b)
    eye_a = jnp.eye(n_a, dtype=jnp.bool_).reshape(1, 1, n_a, n_a, 1)
    w1t = jnp.where(eye_a, bf, jnp.zeros((), bf.dtype))
    w1t = w1t.reshape(n_ch * m_l * n_a, n_a * n_b)
    n_m2, n_p, n_a2 = block_second.shape
    a_l = n_a2 // n_ch
    bs = block_second.reshape(n_m2, n_p, n_ch, a_l)
    bs = jnp.transpose(bs, (2, 0, 3, 1))
    bs = bs.reshape(n_ch, n_m2, a_l, 1, n_p)
    eye_m = jnp.eye(n_m2, dtype=jnp.bool_).reshape(1, n_m2, 1, n_m2, 1)
    w2 = jnp.where(eye_m, bs, jnp.zeros((), bs.dtype))
    w2 = w2.reshape(n_ch * n_m2 * a_l, n_m2 * n_p)
    return w1t, w2


def first_kernel(f_ref, x_ref, tw_ref, o_ref):
    tw = tw_ref[...]
    for i in range(x_ref.shape[0]):
        acc = jnp.dot(f_ref[...], x_ref[i], preferred_element_type=jnp.float32)
        o_ref[:, i, :] = (acc * tw[:, i:i + 1]).astype(o_ref.dtype)


def first_twisted(full_first, token_grid, twiddle_t):
    outer, inner, chans = token_grid.shape
    rows = full_first.shape[0]
    return pl.pallas_call(
        first_kernel,
        out_shape=jax.ShapeDtypeStruct((rows, outer, chans), jnp.bfloat16),
    )(full_first, token_grid, twiddle_t)


def second_kernel(s_ref, g_ref, o_ref):
    srcs, subs, inner, chans = g_ref.shape
    for k in range(subs):
        g = g_ref[:, k, :, :].astype(jnp.float32).reshape(srcs * inner, chans)
        acc = jnp.dot(s_ref[...], g.astype(jnp.bfloat16), preferred_element_type=jnp.float32)
        o_ref[:, k, :] = acc.astype(o_ref.dtype)


def second_mixed(full_second, gathered):
    srcs, subs, inner, chans = gathered.shape
    rows = full_second.shape[0]
    return pl.pallas_call(
        second_kernel,
        out_shape=jax.ShapeDtypeStruct((rows, subs, chans), jnp.bfloat16),
    )(full_second, gathered)


def make_local(n_seq, n_ch):
    def local(inputs, first_factor, twiddle, second_factor, block_first, block_second):
        tok_rows, channels = inputs.shape
        outer_rows = tok_rows // BLOCK
        token_grid = inputs.reshape(outer_rows, BLOCK, channels)
        rows = first_factor.shape[0]
        pair = jnp.concatenate([first_factor, second_factor], axis=0)
        spread = jnp.broadcast_to(pair[None], (n_ch,) + pair.shape)
        both = lax.all_to_all(spread, "ch", split_axis=0, concat_axis=0, tiled=True)
        both = both.reshape(n_ch, 2, rows, BLOCK)
        full_first = both[:, 0].reshape(BLOCK, BLOCK)
        full_second = both[:, 1].reshape(BLOCK, BLOCK)
        twiddle_t = jnp.transpose(twiddle)
        w1t, w2 = channel_weights(block_first, block_second, n_ch)
        contract = (((1,), (1,)), ((), ()))
        width = BLOCK // CHUNKS
        outs = []
        for q in range(CHUNKS):
            lo = q * width
            twisted = first_twisted(full_first[lo:lo + width], token_grid, twiddle_t)
            gathered = lax.all_to_all(twisted, "seq", split_axis=0, concat_axis=0, tiled=True)
            gathered = gathered.reshape(n_seq, width // n_seq, outer_rows, channels)
            mixed = second_mixed(full_second, gathered)
            returned = lax.all_to_all(mixed, "seq", split_axis=0, concat_axis=1, tiled=True)
            gated = (
                token_grid[:, lo:lo + width].astype(jnp.float32) * returned.astype(jnp.float32)
            ).astype(jnp.bfloat16)
            gated = gated.reshape(outer_rows * width, channels)
            middle_t = lax.dot_general(
                w1t, gated, contract, preferred_element_type=jnp.float32
            ).astype(jnp.bfloat16)
            middle_t = middle_t.reshape(n_ch, channels // n_ch, outer_rows * width)
            recv = lax.all_to_all(middle_t, "ch", split_axis=0, concat_axis=0, tiled=True)
            recv = recv.reshape(channels, outer_rows * width)
            result = lax.dot_general(
                recv, w2, (((0,), (0,)), ((), ())), preferred_element_type=jnp.float32
            ).astype(jnp.bfloat16)
            outs.append(result.reshape(outer_rows, width, channels))
        out = jnp.concatenate(outs, axis=1)
        return out.reshape(tok_rows, channels)

    return local


def solution(mesh):
    placed = (
        P("seq", "ch"),
        P("ch", None),
        P("seq", None),
        P("ch", None),
        P("ch", None, None),
        P("ch", None, None),
    )
    return jax.shard_map(
        make_local(mesh.shape["seq"], mesh.shape["ch"]),
        mesh=mesh,
        in_specs=placed,
        out_specs=P("seq", "ch"),
        check_vma=False,
    )
```

```python
import jax
import jax.numpy as jnp
from jax import lax
from jax.sharding import PartitionSpec as P

BLOCK = 512
CHUNKS = 1


def channel_weights(block_first, block_second, n_ch):
    n_a, n_m, n_b = block_first.shape
    m_l = n_m // n_ch
    bf = jnp.transpose(block_first, (1, 0, 2))
    bf = bf.reshape(n_ch, m_l, n_a, 1, n_b)
    eye_a = jnp.eye(n_a, dtype=jnp.bool_).reshape(1, 1, n_a, n_a, 1)
    w1t = jnp.where(eye_a, bf, jnp.zeros((), bf.dtype))
    w1t = w1t.reshape(n_ch * m_l * n_a, n_a * n_b)
    n_m2, n_p, n_a2 = block_second.shape
    a_l = n_a2 // n_ch
    bs = block_second.reshape(n_m2, n_p, n_ch, a_l)
    bs = jnp.transpose(bs, (2, 0, 3, 1))
    bs = bs.reshape(n_ch, n_m2, a_l, 1, n_p)
    eye_m = jnp.eye(n_m2, dtype=jnp.bool_).reshape(1, n_m2, 1, n_m2, 1)
    w2 = jnp.where(eye_m, bs, jnp.zeros((), bs.dtype))
    w2 = w2.reshape(n_ch * n_m2 * a_l, n_m2 * n_p)
    return w1t, w2


def make_local(n_seq, n_ch):
    def local(inputs, first_factor, twiddle, second_factor, block_first, block_second):
        tok_rows, channels = inputs.shape
        outer_rows = tok_rows // BLOCK
        token_grid = inputs.reshape(outer_rows, BLOCK, channels)
        rows = first_factor.shape[0]
        pair = jnp.concatenate([first_factor, second_factor], axis=0)
        spread = jnp.broadcast_to(pair[None], (n_ch,) + pair.shape)
        both = lax.all_to_all(spread, "ch", split_axis=0, concat_axis=0, tiled=True)
        both = both.reshape(n_ch, 2, rows, BLOCK)
        full_first = both[:, 0].reshape(BLOCK, BLOCK)
        full_second = both[:, 1].reshape(BLOCK, BLOCK)
        twiddle_t = jnp.transpose(twiddle)
        token_f32 = lax.optimization_barrier(token_grid.astype(jnp.float32))
        w1t, w2 = channel_weights(block_first, block_second, n_ch)
        contract = (((1,), (1,)), ((), ()))
        width = BLOCK // CHUNKS
        outs = []
        for q in range(CHUNKS):
            lo = q * width
            first = lax.dot_general(
                full_first[lo:lo + width],
                token_grid,
                contract,
                preferred_element_type=jnp.float32,
            )
            twisted = (first * twiddle_t[lo:lo + width, :, None]).astype(jnp.bfloat16)
            gathered = lax.all_to_all(twisted, "seq", split_axis=0, concat_axis=1, tiled=True)
            mixed = lax.dot_general(
                full_second, gathered, contract, preferred_element_type=jnp.float32
            ).astype(jnp.bfloat16)
            returned = lax.all_to_all(mixed, "seq", split_axis=0, concat_axis=1, tiled=True)
            gated = (
                token_f32[:, lo:lo + width] * returned.astype(jnp.float32)
            ).astype(jnp.bfloat16)
            gated = gated.reshape(outer_rows * width, channels)
            middle_t = lax.dot_general(
                w1t, gated, contract, preferred_element_type=jnp.float32
            ).astype(jnp.bfloat16)
            middle_t = middle_t.reshape(n_ch, channels // n_ch, outer_rows * width)
            recv = lax.all_to_all(middle_t, "ch", split_axis=0, concat_axis=0, tiled=True)
            recv = recv.reshape(channels, outer_rows * width)
            result = lax.dot_general(
                recv, w2, (((0,), (0,)), ((), ())), preferred_element_type=jnp.float32
            ).astype(jnp.bfloat16)
            outs.append(result.reshape(outer_rows, width, channels))
        out = jnp.concatenate(outs, axis=1)
        return out.reshape(tok_rows, channels)

    return local


def solution(mesh):
    placed = (
        P("seq", "ch"),
        P("ch", None),
        P("seq", None),
        P("ch", None),
        P("ch", None, None),
        P("ch", None, None),
    )
    return jax.shard_map(
        make_local(mesh.shape["seq"], mesh.shape["ch"]),
        mesh=mesh,
        in_specs=placed,
        out_specs=P("seq", "ch"),
        check_vma=False,
    )
```

```python
import jax
import jax.numpy as jnp
from jax import lax
from jax.sharding import PartitionSpec as P

BLOCK = 512
CHUNKS = 1


def channel_weights(block_first, block_second, n_ch):
    n_a, n_m, n_b = block_first.shape
    m_l = n_m // n_ch
    bf = jnp.transpose(block_first, (1, 0, 2))
    bf = bf.reshape(n_ch, m_l, n_a, 1, n_b)
    eye_a = jnp.eye(n_a, dtype=jnp.bool_).reshape(1, 1, n_a, n_a, 1)
    w1t = jnp.where(eye_a, bf, jnp.zeros((), bf.dtype))
    w1t = w1t.reshape(n_ch * m_l * n_a, n_a * n_b)
    n_m2, n_p, n_a2 = block_second.shape
    a_l = n_a2 // n_ch
    bs = block_second.reshape(n_m2, n_p, n_ch, a_l)
    bs = jnp.transpose(bs, (2, 0, 3, 1))
    bs = bs.reshape(n_ch, n_m2, a_l, 1, n_p)
    eye_m = jnp.eye(n_m2, dtype=jnp.bool_).reshape(1, n_m2, 1, n_m2, 1)
    w2 = jnp.where(eye_m, bs, jnp.zeros((), bs.dtype))
    w2 = w2.reshape(n_ch * n_m2 * a_l, n_m2 * n_p)
    return w1t, w2


def make_local(n_seq, n_ch):
    def local(inputs, first_factor, twiddle, second_factor, block_first, block_second):
        tok_rows, channels = inputs.shape
        outer_rows = tok_rows // BLOCK
        token_grid = inputs.reshape(outer_rows, BLOCK, channels)
        rows = first_factor.shape[0]
        pair = jnp.concatenate([first_factor, second_factor], axis=0)
        spread = jnp.broadcast_to(pair[None], (n_ch,) + pair.shape)
        both = lax.all_to_all(spread, "ch", split_axis=0, concat_axis=0, tiled=True)
        both = both.reshape(n_ch, 2, rows, BLOCK)
        full_first = both[:, 0].reshape(BLOCK, BLOCK)
        full_second = both[:, 1].reshape(BLOCK, BLOCK)
        twiddle_t = jnp.transpose(twiddle)
        token_f32 = lax.optimization_barrier(token_grid)
        w1t, w2 = channel_weights(block_first, block_second, n_ch)
        contract = (((1,), (1,)), ((), ()))
        width = BLOCK // CHUNKS
        outs = []
        for q in range(CHUNKS):
            lo = q * width
            first = lax.dot_general(
                full_first[lo:lo + width],
                token_grid,
                contract,
                preferred_element_type=jnp.float32,
            )
            twisted = (first * twiddle_t[lo:lo + width, :, None]).astype(jnp.bfloat16)
            gathered = lax.all_to_all(twisted, "seq", split_axis=0, concat_axis=1, tiled=True)
            mixed = lax.dot_general(
                full_second, gathered, contract, preferred_element_type=jnp.float32
            ).astype(jnp.bfloat16)
            returned = lax.all_to_all(mixed, "seq", split_axis=0, concat_axis=1, tiled=True)
            gated = (
                token_f32[:, lo:lo + width].astype(jnp.float32) * returned.astype(jnp.float32)
            ).astype(jnp.bfloat16)
            gated = gated.reshape(outer_rows * width, channels)
            middle_t = lax.dot_general(
                w1t, gated, contract, preferred_element_type=jnp.float32
            ).astype(jnp.bfloat16)
            middle_t = middle_t.reshape(n_ch, channels // n_ch, outer_rows * width)
            recv = lax.all_to_all(middle_t, "ch", split_axis=0, concat_axis=0, tiled=True)
            recv = recv.reshape(channels, outer_rows * width)
            result = lax.dot_general(
                recv, w2, (((0,), (0,)), ((), ())), preferred_element_type=jnp.float32
            ).astype(jnp.bfloat16)
            outs.append(result.reshape(outer_rows, width, channels))
        out = jnp.concatenate(outs, axis=1)
        return out.reshape(tok_rows, channels)

    return local


def solution(mesh):
    placed = (
        P("seq", "ch"),
        P("ch", None),
        P("seq", None),
        P("ch", None),
        P("ch", None, None),
        P("ch", None, None),
    )
    return jax.shard_map(
        make_local(mesh.shape["seq"], mesh.shape["ch"]),
        mesh=mesh,
        in_specs=placed,
        out_specs=P("seq", "ch"),
        check_vma=False,
    )
```

```python
import jax
import jax.numpy as jnp
from jax import lax
from jax.sharding import PartitionSpec as P

BLOCK = 512
CHUNKS = 1


def channel_weights(block_first, block_second, n_ch):
    n_a, n_m, n_b = block_first.shape
    m_l = n_m // n_ch
    bf = jnp.transpose(block_first, (1, 0, 2))
    bf = bf.reshape(n_ch, m_l, n_a, 1, n_b)
    eye_a = jnp.eye(n_a, dtype=jnp.bool_).reshape(1, 1, n_a, n_a, 1)
    w1t = jnp.where(eye_a, bf, jnp.zeros((), bf.dtype))
    w1t = w1t.reshape(n_ch * m_l * n_a, n_a * n_b)
    n_m2, n_p, n_a2 = block_second.shape
    a_l = n_a2 // n_ch
    bs = block_second.reshape(n_m2, n_p, n_ch, a_l)
    bs = jnp.transpose(bs, (2, 0, 3, 1))
    bs = bs.reshape(n_ch, n_m2, a_l, 1, n_p)
    eye_m = jnp.eye(n_m2, dtype=jnp.bool_).reshape(1, n_m2, 1, n_m2, 1)
    w2 = jnp.where(eye_m, bs, jnp.zeros((), bs.dtype))
    w2 = w2.reshape(n_ch * n_m2 * a_l, n_m2 * n_p)
    return w1t, w2


def make_local(n_seq, n_ch):
    def local(inputs, first_factor, twiddle, second_factor, block_first, block_second):
        tok_rows, channels = inputs.shape
        outer_rows = tok_rows // BLOCK
        token_grid = inputs.reshape(outer_rows, BLOCK, channels)
        rows = first_factor.shape[0]
        pair = jnp.concatenate([first_factor, second_factor], axis=0)
        spread = jnp.broadcast_to(pair[None], (n_ch,) + pair.shape)
        both = lax.all_to_all(spread, "ch", split_axis=0, concat_axis=0, tiled=True)
        both = both.reshape(n_ch, 2, rows, BLOCK)
        full_first = both[:, 0].reshape(BLOCK, BLOCK)
        full_second = both[:, 1].reshape(BLOCK, BLOCK)
        twiddle_t = jnp.transpose(twiddle)
        token_f32 = lax.optimization_barrier(token_grid)
        w1t, w2 = channel_weights(block_first, block_second, n_ch)
        contract = (((1,), (1,)), ((), ()))
        width = BLOCK // CHUNKS
        outs = []
        for q in range(CHUNKS):
            lo = q * width
            first = lax.dot_general(
                full_first[lo:lo + width],
                token_grid,
                contract,
                preferred_element_type=jnp.float32,
            )
            twisted = (first * twiddle_t[lo:lo + width, :, None]).astype(jnp.bfloat16)
            twisted, w1t, w2 = lax.optimization_barrier((twisted, w1t, w2))
            gathered = lax.all_to_all(twisted, "seq", split_axis=0, concat_axis=1, tiled=True)
            mixed = lax.dot_general(
                full_second, gathered, contract, preferred_element_type=jnp.float32
            ).astype(jnp.bfloat16)
            returned = lax.all_to_all(mixed, "seq", split_axis=0, concat_axis=1, tiled=True)
            gated = (
                token_f32[:, lo:lo + width].astype(jnp.float32) * returned.astype(jnp.float32)
            ).astype(jnp.bfloat16)
            gated = gated.reshape(outer_rows * width, channels)
            middle_t = lax.dot_general(
                w1t, gated, contract, preferred_element_type=jnp.float32
            ).astype(jnp.bfloat16)
            middle_t = middle_t.reshape(n_ch, channels // n_ch, outer_rows * width)
            recv = lax.all_to_all(middle_t, "ch", split_axis=0, concat_axis=0, tiled=True)
            recv = recv.reshape(channels, outer_rows * width)
            result = lax.dot_general(
                recv, w2, (((0,), (0,)), ((), ())), preferred_element_type=jnp.float32
            ).astype(jnp.bfloat16)
            outs.append(result.reshape(outer_rows, width, channels))
        out = jnp.concatenate(outs, axis=1)
        return out.reshape(tok_rows, channels)

    return local


def solution(mesh):
    placed = (
        P("seq", "ch"),
        P("ch", None),
        P("seq", None),
        P("ch", None),
        P("ch", None, None),
        P("ch", None, None),
    )
    return jax.shard_map(
        make_local(mesh.shape["seq"], mesh.shape["ch"]),
        mesh=mesh,
        in_specs=placed,
        out_specs=P("seq", "ch"),
        check_vma=False,
    )
```
